512 devices in a mesh: row: 32 (over z_hi, x, core), col: 16 (over z_lo, y).
Axes of the slice: x: 4, y: 8, z: 8 (z_hi: 4, z_lo: 2; z = z_hi * 2 + z_lo), core: 2. Of those that a mesh axis runs over, the one named last changes fastest.
Arguments:
- embeddings: float32 [16384, 768], P(('row', 'col')), may hold values from -0.21650635 to 0.21650635
- sharpness: float32 [16384], P(('row', 'col')), may hold values from 0.5 to 4
- soft_labels: float32 [16384, 256], P(('row', 'col')), may hold values from 0 to 1
- seed_mask: int32 [16384], P(('row', 'col')), may hold values 0 or 1
- tile_mask: int32 [512, 512], P('row'), may hold values from 0 to 1, as said below
Outputs:
- spread_labels: float32 [16384, 256], P(('row', 'col'))
The draws below stay inside these ranges and needn't reach their ends.
Inputs may be any that keep to these rules, and one draw needn't show every extreme that they name: Every diagonal entry tile_mask[p, p] is 1.
All inputs are finite; a program needn't handle non-finite values. No bound on the sum of `seed_mask` on one device may be relied on, other than what follows from the above.
Results may differ from the reference program's by a relative error of at most 0.0003.
Values sent between devices are 32-bit elements; how exact they have to be, the bound alone decides.
No kernel may reach another device: no remote copies, remote signals or barrier semaphores. Data moves between devices by JAX's collectives and lax.ppermute only.
A program may use at most 64 MiB of HBM per device.

```python
import math
import jax
import jax.numpy as jnp
from jax import lax

E = 768
LABELS = 256
PIECE = 32
ITERS = 3
PIECES = 512
DOCS = 16384
N_ROW = 32


def draw_tile_mask(key, part):
    key_rate, key_roll = jax.random.split(jax.random.fold_in(key, 17))
    density = jax.random.randint(key_rate, (PIECES, 1), 10, 26)
    rolled = jax.random.randint(key_roll, (PIECES, PIECES), 0, 100)
    diagonal = jnp.arange(PIECES)[:, None] == jnp.arange(PIECES)[None, :]
    return jnp.where(diagonal | (rolled < density), 1, 0).astype(jnp.int32)


def plant(drawn, stream_key, smallest, high):
    extent = drawn.shape
    place = [jax.random.randint(jax.random.fold_in(stream_key, axis), (), 0, extent[axis]) for axis in range(len(extent))]
    drawn = drawn.at[tuple(place)].set(smallest)
    longest = extent.index(max(extent))
    place[longest] = (place[longest] + 1) % extent[longest]
    return drawn.at[tuple(place)].set(high)


def block_scale(rng, shape, cuts, smallest, top_value):
    loudness = 1.0
    for axis_at, blocks in cuts:
        steps = jax.random.uniform(jax.random.fold_in(jax.random.fold_in(rng, 6), axis_at), (blocks,), jnp.float32, smallest / len(cuts), top_value / len(cuts))
        loudness = loudness * jnp.repeat(jnp.exp(steps), shape[axis_at] // blocks).reshape((-1,) + (1,) * (len(shape) - 1 - axis_at))
    return loudness


def centred(stream_key, dims, width, bound, pieces=(), kind=jnp.bfloat16):
    array = jax.random.normal(stream_key, dims, jnp.float32) * width
    if len(pieces) > 0:
        array = block_scale(stream_key, dims, pieces, -0.22, 0.18) * array
    return jnp.clip(array, min=-bound, max=bound).astype(kind)


def setup_inputs(seed: int = 0) -> dict:
    keys = jax.random.split(jax.random.key(seed), 6)
    embeddings = centred(keys[0], (DOCS, E), (E ** -0.5), 0.21650635, ((0, 512),), jnp.float32)
    sharpness = jnp.clip(jnp.exp(math.log(4.0) - 2.0794415 * jax.random.uniform(keys[1], (DOCS,), jnp.float32) ** block_scale(keys[1], (DOCS,), ((0, 512),), -0.2, 0.2)), 0.5, 4.0)
    soft_labels = jnp.clip(1.0 * jax.random.uniform(keys[2], (DOCS, LABELS), jnp.float32) ** block_scale(keys[2], (DOCS, LABELS), ((0, 512),), -0.2, 0.2), 0.0, 1.0)
    seed_mask = plant((jax.random.randint(keys[3], (DOCS,), 0, 4) < 1).astype(jnp.int32), jax.random.fold_in(keys[3], 1), 0, 1)
    tile_mask = draw_tile_mask(jax.random.fold_in(keys[5], 71), 0)
    return dict(embeddings=embeddings, sharpness=sharpness, soft_labels=soft_labels, seed_mask=seed_mask, tile_mask=tile_mask)


def reference(embeddings, sharpness, soft_labels, seed_mask, tile_mask):
    seeded = seed_mask.astype(jnp.float32)[:, None] * soft_labels
    squares = jnp.sum(embeddings * embeddings, axis=1)
    block_rows = DOCS // N_ROW
    piece_rows = block_rows // PIECE

    def block_update(labels, index):
        start = (index * block_rows).astype(jnp.int32)
        rows = lax.dynamic_slice_in_dim(embeddings, start, block_rows, 0)
        row_squares = lax.dynamic_slice_in_dim(squares, start, block_rows, 0)
        row_width = lax.dynamic_slice_in_dim(sharpness, start, block_rows, 0)
        piece_mask = lax.dynamic_slice_in_dim(tile_mask, (index * piece_rows).astype(jnp.int32), piece_rows, 0)
        full_mask = jnp.broadcast_to(piece_mask[:, None, :, None], (piece_rows, PIECE, PIECES, PIECE))
        full_mask = full_mask.reshape(block_rows, DOCS).astype(jnp.float32)
        cross = jnp.dot(rows, embeddings.T, precision=lax.Precision.HIGHEST, preferred_element_type=jnp.float32)
        distance = row_squares[:, None] + squares[None, :] - 2.0 * cross
        weights = jnp.exp(-(distance * row_width[:, None] * sharpness[None, :])) * full_mask
        partial_value = jnp.dot(weights, labels, precision=lax.Precision.HIGHEST, preferred_element_type=jnp.float32)
        return partial_value, jnp.sum(weights, axis=1)

    labels = seeded
    for iteration in range(ITERS):
        partial_value, degree = lax.map(lambda index: block_update(labels, index), jnp.arange(N_ROW, dtype=jnp.int32))
        partial_value = partial_value.reshape(DOCS, LABELS)
        degree = degree.reshape(DOCS)
        labels = 0.9 * partial_value / degree[:, None] + 0.1 * seeded
    return labels
```

```python
import jax
import jax.numpy as jnp
from jax import lax
from jax.sharding import PartitionSpec as P

ITERS = 3


def gather_rows(x, axis, n):
    copies = jnp.broadcast_to(x[None], (n,) + x.shape)
    got = lax.all_to_all(copies, axis, 0, 0, tiled=False)
    return got.reshape((n * x.shape[0],) + x.shape[1:])


def scatter_sum(p, axis, n):
    chunk = p.shape[0] // n
    got = lax.all_to_all(p.reshape((n, chunk) + p.shape[1:]), axis, 0, 0, tiled=False)
    return jnp.sum(got, axis=0)


def local(embeddings, sharpness, soft_labels, seed_mask, tile_mask):
    n_row = lax.axis_size("row")
    n_col = lax.axis_size("col")
    col_index = lax.axis_index("col")
    piece, width = embeddings.shape
    n_labels = soft_labels.shape[1]
    seeded = seed_mask.astype(jnp.float32)[:, None] * soft_labels
    squares = jnp.sum(embeddings * embeddings, axis=1)
    packed = jnp.concatenate([embeddings, sharpness[:, None], squares[:, None]], axis=1)
    row_pack = gather_rows(packed, "col", n_col)
    col_pack = gather_rows(jnp.concatenate([packed, seeded], axis=1), "row", n_row)
    row_emb, row_width, row_squares = row_pack[:, :width], row_pack[:, width], row_pack[:, width + 1]
    col_emb, col_width, col_squares = col_pack[:, :width], col_pack[:, width], col_pack[:, width + 1]
    col_labels = col_pack[:, width + 2:]
    block_rows = row_emb.shape[0]
    col_rows = piece * n_row
    grouped = tile_mask.reshape(n_col, n_row, n_col)
    chosen = lax.dynamic_index_in_dim(grouped, col_index, axis=2, keepdims=False)
    col_mask = jnp.broadcast_to(chosen[:, None, :, None], (n_col, piece, n_row, piece))
    col_mask = col_mask.reshape(block_rows, col_rows).astype(jnp.float32)
    cross = jnp.dot(row_emb, col_emb.T, precision=lax.Precision.HIGHEST, preferred_element_type=jnp.float32)
    distance = row_squares[:, None] + col_squares[None, :] - 2.0 * cross
    weights = jnp.exp(-(distance * row_width[:, None] * col_width[None, :])) * col_mask
    degree = None
    labels = seeded
    for iteration in range(ITERS):
        if iteration > 0:
            col_labels = gather_rows(labels, "row", n_row)
        partial_value = jnp.dot(
            weights, col_labels, precision=lax.Precision.HIGHEST, preferred_element_type=jnp.float32
        )
        if degree is None:
            both = jnp.concatenate([partial_value, jnp.sum(weights, axis=1)[:, None]], axis=1)
            both = scatter_sum(both, "col", n_col)
            own_part, degree = both[:, :n_labels], both[:, n_labels]
        else:
            own_part = scatter_sum(partial_value, "col", n_col)
        labels = 0.9 * own_part / degree[:, None] + 0.1 * seeded
    return labels


def solution(mesh):
    return jax.shard_map(
        local,
        mesh=mesh,
        in_specs=(
            P(("row", "col"), None),
            P(("row", "col")),
            P(("row", "col"), None),
            P(("row", "col")),
            P("row", None),
        ),
        out_specs=P(("row", "col"), None),
        check_vma=False,
    )
```

```python
import jax
import jax.numpy as jnp
from jax import lax
from jax.sharding import Mesh
from jax.sharding import PartitionSpec as P

ITERS = 3
CHIPS = ("zh", "x")
DOCS = ("zh", "x", "core", "col")


def gather_rows(x, axis, n):
    copies = jnp.broadcast_to(x[None], (n,) + x.shape)
    got = lax.all_to_all(copies, axis, 0, 0, tiled=False)
    return got.reshape((n * x.shape[0],) + x.shape[1:])


def gather_row_set(x, n_chips):
    mine = gather_rows(x, CHIPS, n_chips)
    other = lax.ppermute(mine, "core", [(0, 1), (1, 0)])
    return jnp.concatenate([mine, other], axis=0)


def scatter_sum(p, axis, n):
    chunk = p.shape[0] // n
    got = lax.all_to_all(p.reshape((n, chunk) + p.shape[1:]), axis, 0, 0, tiled=False)
    return jnp.sum(got, axis=0)


def local(embeddings, sharpness, soft_labels, seed_mask, tile_mask):
    n_chips = lax.axis_size(CHIPS)
    n_col = lax.axis_size("col")
    col_index = lax.axis_index("col")
    core = lax.axis_index("core")
    piece, width = embeddings.shape
    n_labels = soft_labels.shape[1]
    seeded = seed_mask.astype(jnp.float32)[:, None] * soft_labels
    squares = jnp.sum(embeddings * embeddings, axis=1)
    packed = jnp.concatenate([embeddings, sharpness[:, None], squares[:, None]], axis=1)
    row_pack = gather_rows(packed, "col", n_col)
    col_pack = gather_row_set(jnp.concatenate([packed, seeded], axis=1), n_chips)
    row_emb, row_width, row_squares = row_pack[:, :width], row_pack[:, width], row_pack[:, width + 1]
    col_emb, col_width, col_squares = col_pack[:, :width], col_pack[:, width], col_pack[:, width + 1]
    col_labels = col_pack[:, width + 2:]
    block_rows = row_emb.shape[0]
    col_rows = col_emb.shape[0]
    grouped = tile_mask.reshape(n_col, n_chips, 2, n_col)
    chosen = lax.dynamic_index_in_dim(grouped, col_index, axis=3, keepdims=False)
    own_half = lax.dynamic_index_in_dim(chosen, core, axis=2, keepdims=False)
    other_half = lax.dynamic_index_in_dim(chosen, 1 - core, axis=2, keepdims=False)
    chosen = jnp.concatenate([own_half, other_half], axis=1)
    col_mask = jnp.broadcast_to(chosen[:, None, :, None], (n_col, piece, 2 * n_chips, piece))
    col_mask = col_mask.reshape(block_rows, col_rows).astype(jnp.float32)
    cross = jnp.dot(row_emb, col_emb.T, precision=lax.Precision.HIGHEST, preferred_element_type=jnp.float32)
    distance = row_squares[:, None] + col_squares[None, :] - 2.0 * cross
    weights = jnp.exp(-(distance * row_width[:, None] * col_width[None, :])) * col_mask
    degree = None
    labels = seeded
    for iteration in range(ITERS):
        if iteration > 0:
            col_labels = gather_row_set(labels, n_chips)
        partial_value = jnp.dot(
            weights, col_labels, precision=lax.Precision.HIGHEST, preferred_element_type=jnp.float32
        )
        if degree is None:
            both = jnp.concatenate([partial_value, jnp.sum(weights, axis=1)[:, None]], axis=1)
            both = scatter_sum(both, "col", n_col)
            own_part, degree = both[:, :n_labels], both[:, n_labels]
        else:
            own_part = scatter_sum(partial_value, "col", n_col)
        labels = 0.9 * own_part / degree[:, None] + 0.1 * seeded
    return labels


def solution(mesh):
    n_row, n_col = mesh.devices.shape
    fine = Mesh(mesh.devices.reshape(n_row // 8, 4, 2, n_col), DOCS)
    return jax.shard_map(
        local,
        mesh=fine,
        in_specs=(
            P(DOCS, None),
            P(DOCS),
            P(DOCS, None),
            P(DOCS),
            P(("zh", "x", "core"), None),
        ),
        out_specs=P(DOCS, None),
        check_vma=False,
    )
```

```python
import jax
import jax.numpy as jnp
from jax import lax
from jax.sharding import Mesh
from jax.sharding import PartitionSpec as P

ITERS = 3
CHIPS = ("zh", "x")
DOCS = ("zh", "x", "core", "col")


def gather_rows(x, axis, n):
    copies = jnp.broadcast_to(x[None], (n,) + x.shape)
    got = lax.all_to_all(copies, axis, 0, 0, tiled=False)
    return got.reshape((n * x.shape[0],) + x.shape[1:])


def gather_row_set(x, n_chips):
    mine = gather_rows(x, CHIPS, n_chips)
    other = lax.ppermute(mine, "core", [(0, 1), (1, 0)])
    return jnp.concatenate([mine, other], axis=0)


def scatter_sum(p, axis, n):
    chunk = p.shape[0] // n
    got = lax.all_to_all(p.reshape((n, chunk) + p.shape[1:]), axis, 0, 0, tiled=False)
    return jnp.sum(got, axis=0)


def local(embeddings, sharpness, soft_labels, seed_mask, tile_mask):
    n_chips = lax.axis_size(CHIPS)
    n_col = lax.axis_size("col")
    col_index = lax.axis_index("col")
    core = lax.axis_index("core")
    piece, width = embeddings.shape
    n_labels = soft_labels.shape[1]
    seeded = seed_mask.astype(jnp.float32)[:, None] * soft_labels
    squares = jnp.sum(embeddings * embeddings, axis=1)
    packed = jnp.concatenate([embeddings, sharpness[:, None], squares[:, None]], axis=1)
    row_pack = lax.all_gather(packed, "col", axis=0, tiled=True)
    col_pack = gather_row_set(jnp.concatenate([packed, seeded], axis=1), n_chips)
    row_emb, row_width, row_squares = row_pack[:, :width], row_pack[:, width], row_pack[:, width + 1]
    col_emb, col_width, col_squares = col_pack[:, :width], col_pack[:, width], col_pack[:, width + 1]
    col_labels = col_pack[:, width + 2:]
    block_rows = row_emb.shape[0]
    col_rows = col_emb.shape[0]
    grouped = tile_mask.reshape(n_col, n_chips, 2, n_col)
    chosen = lax.dynamic_index_in_dim(grouped, col_index, axis=3, keepdims=False)
    own_half = lax.dynamic_index_in_dim(chosen, core, axis=2, keepdims=False)
    other_half = lax.dynamic_index_in_dim(chosen, 1 - core, axis=2, keepdims=False)
    chosen = jnp.concatenate([own_half, other_half], axis=1)
    col_mask = jnp.broadcast_to(chosen[:, None, :, None], (n_col, piece, 2 * n_chips, piece))
    col_mask = col_mask.reshape(block_rows, col_rows).astype(jnp.float32)
    cross = jnp.dot(row_emb, col_emb.T, precision=lax.Precision.HIGHEST, preferred_element_type=jnp.float32)
    distance = row_squares[:, None] + col_squares[None, :] - 2.0 * cross
    weights = jnp.exp(-(distance * row_width[:, None] * col_width[None, :])) * col_mask
    degree = None
    labels = seeded
    for iteration in range(ITERS):
        if iteration > 0:
            col_labels = gather_row_set(labels, n_chips)
        partial_value = jnp.dot(
            weights, col_labels, precision=lax.Precision.HIGHEST, preferred_element_type=jnp.float32
        )
        if degree is None:
            both = jnp.concatenate([partial_value, jnp.sum(weights, axis=1)[:, None]], axis=1)
            both = scatter_sum(both, "col", n_col)
            own_part, degree = both[:, :n_labels], both[:, n_labels]
        else:
            own_part = scatter_sum(partial_value, "col", n_col)
        labels = 0.9 * own_part / degree[:, None] + 0.1 * seeded
    return labels


def solution(mesh):
    n_row, n_col = mesh.devices.shape
    fine = Mesh(mesh.devices.reshape(n_row // 8, 4, 2, n_col), DOCS)
    return jax.shard_map(
        local,
        mesh=fine,
        in_specs=(
            P(DOCS, None),
            P(DOCS),
            P(DOCS, None),
            P(DOCS),
            P(("zh", "x", "core"), None),
        ),
        out_specs=P(DOCS, None),
        check_vma=False,
    )
```

```python
import jax
import jax.numpy as jnp
from jax import lax
from jax.sharding import Mesh
from jax.sharding import PartitionSpec as P

ITERS = 3
CHIPS = ("zh", "x")
DOCS = ("zh", "x", "core", "col")


def gather_rows(x, axis, n):
    copies = jnp.broadcast_to(x[None], (n,) + x.shape)
    got = lax.all_to_all(copies, axis, 0, 0, tiled=False)
    return got.reshape((n * x.shape[0],) + x.shape[1:])


def gather_row_set(x, n_chips):
    copies = jnp.broadcast_to(x[None], (n_chips,) + x.shape)
    mine = lax.all_to_all(copies, CHIPS, 0, 0, tiled=False)
    other = lax.ppermute(mine, "core", [(0, 1), (1, 0)])
    both = jnp.concatenate([mine, other], axis=0)
    return both.reshape((2 * n_chips * x.shape[0],) + x.shape[1:])


def scatter_sum(p, axis, n):
    chunk = p.shape[0] // n
    got = lax.all_to_all(p.reshape((n, chunk) + p.shape[1:]), axis, 0, 0, tiled=False)
    return jnp.sum(got, axis=0)


def local(embeddings, sharpness, soft_labels, seed_mask, tile_mask):
    n_chips = lax.axis_size(CHIPS)
    n_col = lax.axis_size("col")
    col_index = lax.axis_index("col")
    core = lax.axis_index("core")
    piece, width = embeddings.shape
    n_labels = soft_labels.shape[1]
    seeded = seed_mask.astype(jnp.float32)[:, None] * soft_labels
    squares = jnp.sum(embeddings * embeddings, axis=1)
    packed = jnp.concatenate([embeddings, sharpness[:, None], squares[:, None]], axis=1)
    col_pack = gather_row_set(jnp.concatenate([packed, seeded], axis=1), n_chips)
    row_pack = gather_rows(packed, "col", n_col)
    row_emb, row_width, row_squares = row_pack[:, :width], row_pack[:, width], row_pack[:, width + 1]
    col_emb, col_width, col_squares = col_pack[:, :width], col_pack[:, width], col_pack[:, width + 1]
    col_labels = col_pack[:, width + 2:]
    block_rows = row_emb.shape[0]
    col_rows = col_emb.shape[0]
    grouped = tile_mask.reshape(n_col, n_chips, 2, n_col)
    chosen = lax.dynamic_index_in_dim(grouped, col_index, axis=3, keepdims=False)
    own_half = lax.dynamic_index_in_dim(chosen, core, axis=2, keepdims=False)
    other_half = lax.dynamic_index_in_dim(chosen, 1 - core, axis=2, keepdims=False)
    chosen = jnp.concatenate([own_half, other_half], axis=1)
    col_mask = jnp.broadcast_to(chosen[:, None, :, None], (n_col, piece, 2 * n_chips, piece))
    col_mask = col_mask.reshape(block_rows, col_rows).astype(jnp.float32)
    cross = jnp.dot(row_emb, col_emb.T, precision=lax.Precision.HIGHEST, preferred_element_type=jnp.float32)
    distance = row_squares[:, None] + col_squares[None, :] - 2.0 * cross
    weights = jnp.exp(-(distance * row_width[:, None] * col_width[None, :])) * col_mask
    degree = None
    labels = seeded
    for iteration in range(ITERS):
        if iteration > 0:
            col_labels = gather_row_set(labels, n_chips)
        partial_value = jnp.dot(
            weights, col_labels, precision=lax.Precision.HIGHEST, preferred_element_type=jnp.float32
        )
        if degree is None:
            row_sums = jnp.sum(weights, axis=1).reshape(n_col, 1, piece)
            row_sums = jnp.pad(row_sums, ((0, 0), (0, 7), (0, n_labels - piece)))
            both = jnp.concatenate([partial_value.reshape(n_col, piece, n_labels), row_sums], axis=1)
            both = scatter_sum(both.reshape(n_col * (piece + 8), n_labels), "col", n_col)
            own_part, degree = both[:piece], both[piece, :piece]
        else:
            own_part = scatter_sum(partial_value, "col", n_col)
        labels = 0.9 * own_part / degree[:, None] + 0.1 * seeded
    return labels


def solution(mesh):
    n_row, n_col = mesh.devices.shape
    fine = Mesh(mesh.devices.reshape(n_row // 8, 4, 2, n_col), DOCS)
    return jax.shard_map(
        local,
        mesh=fine,
        in_specs=(
            P(DOCS, None),
            P(DOCS),
            P(DOCS, None),
            P(DOCS),
            P(("zh", "x", "core"), None),
        ),
        out_specs=P(DOCS, None),
        check_vma=False,
    )
```

```python
import jax
import jax.numpy as jnp
from jax import lax
from jax.sharding import Mesh
from jax.sharding import PartitionSpec as P

ITERS = 3
CHIPS = ("zh", "x")
DOCS = ("zh", "x", "core", "col")


def gather_rows(x, axis, n):
    copies = jnp.broadcast_to(x[None], (n,) + x.shape)
    got = lax.all_to_all(copies, axis, 0, 0, tiled=False)
    return got.reshape((n * x.shape[0],) + x.shape[1:])


def gather_row_set(x, n_chips):
    copies = jnp.broadcast_to(x[None], (n_chips,) + x.shape)
    mine = lax.all_to_all(copies, CHIPS, 0, 0, tiled=False)
    other = lax.ppermute(mine, "core", [(0, 1), (1, 0)])
    both = jnp.concatenate([mine, other], axis=0)
    return both.reshape((2 * n_chips * x.shape[0],) + x.shape[1:])


def scatter_sum(p, axis, n):
    chunk = p.shape[0] // n
    got = lax.all_to_all(p.reshape((n, chunk) + p.shape[1:]), axis, 0, 0, tiled=False)
    return jnp.sum(got, axis=0)


def local(embeddings, sharpness, soft_labels, seed_mask, tile_mask):
    n_chips = lax.axis_size(CHIPS)
    n_col = lax.axis_size("col")
    col_index = lax.axis_index("col")
    core = lax.axis_index("core")
    piece, width = embeddings.shape
    n_labels = soft_labels.shape[1]
    seeded = seed_mask.astype(jnp.float32)[:, None] * soft_labels
    squares = jnp.sum(embeddings * embeddings, axis=1)
    packed = jnp.concatenate([embeddings, sharpness[:, None], squares[:, None]], axis=1)
    col_pack = lax.all_gather(jnp.concatenate([packed, seeded], axis=1), ("zh", "x", "core"), axis=0, tiled=True)
    row_pack = gather_rows(packed, "col", n_col)
    row_emb, row_width, row_squares = row_pack[:, :width], row_pack[:, width], row_pack[:, width + 1]
    col_emb, col_width, col_squares = col_pack[:, :width], col_pack[:, width], col_pack[:, width + 1]
    col_labels = col_pack[:, width + 2:]
    block_rows = row_emb.shape[0]
    col_rows = col_emb.shape[0]
    grouped = tile_mask.reshape(n_col, 2 * n_chips, n_col)
    chosen = lax.dynamic_index_in_dim(grouped, col_index, axis=2, keepdims=False)
    col_mask = jnp.broadcast_to(chosen[:, None, :, None], (n_col, piece, 2 * n_chips, piece))
    col_mask = col_mask.reshape(block_rows, col_rows).astype(jnp.float32)
    cross = jnp.dot(row_emb, col_emb.T, precision=lax.Precision.HIGHEST, preferred_element_type=jnp.float32)
    distance = row_squares[:, None] + col_squares[None, :] - 2.0 * cross
    weights = jnp.exp(-(distance * row_width[:, None] * col_width[None, :])) * col_mask
    split = weights.reshape(block_rows, n_chips, 2, piece)
    split = jnp.where(core == 0, split, split[:, :, ::-1, :])
    split = jnp.transpose(split, (0, 2, 1, 3)).reshape(block_rows, col_rows)
    degree = None
    labels = seeded
    for iteration in range(ITERS):
        if iteration > 0:
            col_labels = gather_row_set(labels, n_chips)
        partial_value = jnp.dot(
            split if iteration > 0 else weights, col_labels, precision=lax.Precision.HIGHEST, preferred_element_type=jnp.float32
        )
        if degree is None:
            row_sums = jnp.sum(weights, axis=1).reshape(n_col, 1, piece)
            row_sums = jnp.pad(row_sums, ((0, 0), (0, 7), (0, n_labels - piece)))
            both = jnp.concatenate([partial_value.reshape(n_col, piece, n_labels), row_sums], axis=1)
            both = scatter_sum(both.reshape(n_col * (piece + 8), n_labels), "col", n_col)
            own_part, degree = both[:piece], both[piece, :piece]
        else:
            own_part = scatter_sum(partial_value, "col", n_col)
        labels = 0.9 * own_part / degree[:, None] + 0.1 * seeded
    return labels


def solution(mesh):
    n_row, n_col = mesh.devices.shape
    fine = Mesh(mesh.devices.reshape(n_row // 8, 4, 2, n_col), DOCS)
    return jax.shard_map(
        local,
        mesh=fine,
        in_specs=(
            P(DOCS, None),
            P(DOCS),
            P(DOCS, None),
            P(DOCS),
            P(("zh", "x", "core"), None),
        ),
        out_specs=P(DOCS, None),
        check_vma=False,
    )
```

```python
import jax
import jax.numpy as jnp
from jax import lax
from jax.sharding import Mesh
from jax.sharding import PartitionSpec as P

ITERS = 3
CHIPS = ("zh", "x")
DOCS = ("zh", "x", "core", "col")


def gather_rows(x, axis, n):
    copies = jnp.broadcast_to(x[None], (n,) + x.shape)
    got = lax.all_to_all(copies, axis, 0, 0, tiled=False)
    return got.reshape((n * x.shape[0],) + x.shape[1:])


def gather_row_set(x, n_chips):
    copies = jnp.broadcast_to(x[None], (n_chips,) + x.shape)
    mine = lax.all_to_all(copies, CHIPS, 0, 0, tiled=False)
    other = lax.ppermute(mine, "core", [(0, 1), (1, 0)])
    core0 = lax.axis_index("core") == 0
    both = jnp.stack([jnp.where(core0, mine, other), jnp.where(core0, other, mine)], axis=1)
    return both.reshape((2 * n_chips * x.shape[0],) + x.shape[1:])


def scatter_sum(p, axis, n):
    chunk = p.shape[0] // n
    got = lax.all_to_all(p.reshape((n, chunk) + p.shape[1:]), axis, 0, 0, tiled=False)
    return jnp.sum(got, axis=0)


def local(embeddings, sharpness, soft_labels, seed_mask, tile_mask):
    n_chips = lax.axis_size(CHIPS)
    n_col = lax.axis_size("col")
    col_index = lax.axis_index("col")
    piece, width = embeddings.shape
    n_labels = soft_labels.shape[1]
    seeded = seed_mask.astype(jnp.float32)[:, None] * soft_labels
    squares = jnp.sum(embeddings * embeddings, axis=1)
    packed = jnp.concatenate([embeddings, sharpness[:, None], squares[:, None]], axis=1)
    col_pack = lax.all_gather(jnp.concatenate([packed, seeded], axis=1), ("zh", "x", "core"), axis=0, tiled=True)
    row_pack = gather_rows(packed, "col", n_col)
    row_emb, row_width, row_squares = row_pack[:, :width], row_pack[:, width], row_pack[:, width + 1]
    col_emb, col_width, col_squares = col_pack[:, :width], col_pack[:, width], col_pack[:, width + 1]
    col_labels = col_pack[:, width + 2:]
    block_rows = row_emb.shape[0]
    col_rows = col_emb.shape[0]
    grouped = tile_mask.reshape(n_col, 2 * n_chips, n_col)
    chosen = lax.dynamic_index_in_dim(grouped, col_index, axis=2, keepdims=False)
    col_mask = jnp.broadcast_to(chosen[:, None, :, None], (n_col, piece, 2 * n_chips, piece))
    col_mask = col_mask.reshape(block_rows, col_rows).astype(jnp.float32)
    cross = jnp.dot(row_emb, col_emb.T, precision=lax.Precision.HIGHEST, preferred_element_type=jnp.float32)
    distance = row_squares[:, None] + col_squares[None, :] - 2.0 * cross
    weights = jnp.exp(-(distance * row_width[:, None] * col_width[None, :])) * col_mask
    degree = None
    labels = seeded
    for iteration in range(ITERS):
        if iteration > 0:
            col_labels = gather_row_set(labels, n_chips)
        partial_value = jnp.dot(
            weights, col_labels, precision=lax.Precision.HIGHEST, preferred_element_type=jnp.float32
        )
        if degree is None:
            row_sums = jnp.sum(weights, axis=1).reshape(n_col, 1, piece)
            row_sums = jnp.pad(row_sums, ((0, 0), (0, 7), (0, n_labels - piece)))
            both = jnp.concatenate([partial_value.reshape(n_col, piece, n_labels), row_sums], axis=1)
            both = scatter_sum(both.reshape(n_col * (piece + 8), n_labels), "col", n_col)
            own_part, degree = both[:piece], both[piece, :piece]
        else:
            own_part = scatter_sum(partial_value, "col", n_col)
        labels = 0.9 * own_part / degree[:, None] + 0.1 * seeded
    return labels


def solution(mesh):
    n_row, n_col = mesh.devices.shape
    fine = Mesh(mesh.devices.reshape(n_row // 8, 4, 2, n_col), DOCS)
    return jax.shard_map(
        local,
        mesh=fine,
        in_specs=(
            P(DOCS, None),
            P(DOCS),
            P(DOCS, None),
            P(DOCS),
            P(("zh", "x", "core"), None),
        ),
        out_specs=P(DOCS, None),
        check_vma=False,
    )
```

```python
import jax
import jax.numpy as jnp
from jax import lax
from jax.sharding import Mesh
from jax.sharding import PartitionSpec as P

ITERS = 3
CHIPS = ("zh", "x")
DOCS = ("zh", "x", "core", "col")


def gather_rows(x, axis, n):
    copies = jnp.broadcast_to(x[None], (n,) + x.shape)
    got = lax.all_to_all(copies, axis, 0, 0, tiled=False)
    return got.reshape((n * x.shape[0],) + x.shape[1:])


def gather_row_set(x, n_chips):
    copies = jnp.broadcast_to(x[None], (n_chips,) + x.shape)
    mine = lax.all_to_all(copies, CHIPS, 0, 0, tiled=False)
    other = lax.ppermute(mine, "core", [(0, 1), (1, 0)])
    core0 = lax.axis_index("core") == 0
    both = jnp.stack([jnp.where(core0, mine, other), jnp.where(core0, other, mine)], axis=1)
    return both.reshape((2 * n_chips * x.shape[0],) + x.shape[1:])


def scatter_sum(p, axis, n):
    chunk = p.shape[0] // n
    got = lax.all_to_all(p.reshape((n, chunk) + p.shape[1:]), axis, 0, 0, tiled=False)
    return jnp.sum(got, axis=0)


def local(embeddings, sharpness, soft_labels, seed_mask, tile_mask):
    n_chips = lax.axis_size(CHIPS)
    n_col = lax.axis_size("col")
    col_index = lax.axis_index("col")
    piece, width = embeddings.shape
    n_labels = soft_labels.shape[1]
    seeded = seed_mask.astype(jnp.float32)[:, None] * soft_labels
    squares = jnp.sum(embeddings * embeddings, axis=1)
    packed = jnp.concatenate([embeddings, sharpness[:, None], squares[:, None]], axis=1)
    col_pack = lax.all_gather(jnp.concatenate([packed, seeded], axis=1), ("zh", "x", "core"), axis=0, tiled=True)
    row_pack = gather_rows(packed, "col", n_col)
    row_emb, row_width, row_squares = row_pack[:, :width], row_pack[:, width], row_pack[:, width + 1]
    col_emb, col_width, col_squares = col_pack[:, :width], col_pack[:, width], col_pack[:, width + 1]
    col_labels = col_pack[:, width + 2:]
    block_rows = row_emb.shape[0]
    col_rows = col_emb.shape[0]
    grouped = tile_mask.reshape(n_col, 2 * n_chips, n_col)
    chosen = lax.dynamic_index_in_dim(grouped, col_index, axis=2, keepdims=False)
    col_mask = jnp.broadcast_to(chosen[:, None, :, None], (n_col, piece, 2 * n_chips, piece))
    col_mask = col_mask.reshape(block_rows, col_rows).astype(jnp.float32)
    cross = jnp.dot(row_emb, col_emb.T, precision=lax.Precision.HIGHEST, preferred_element_type=jnp.float32)
    distance = row_squares[:, None] + col_squares[None, :] - 2.0 * cross
    weights = jnp.exp(-(distance * row_width[:, None] * col_width[None, :])) * col_mask
    degree = None
    labels = seeded
    for iteration in range(ITERS):
        if iteration > 0:
            col_labels = gather_row_set(labels, n_chips)
        partial_value = jnp.dot(
            weights, col_labels, precision=lax.Precision.HIGH, preferred_element_type=jnp.float32
        )
        if degree is None:
            row_sums = jnp.sum(weights, axis=1).reshape(n_col, 1, piece)
            row_sums = jnp.pad(row_sums, ((0, 0), (0, 7), (0, n_labels - piece)))
            both = jnp.concatenate([partial_value.reshape(n_col, piece, n_labels), row_sums], axis=1)
            both = scatter_sum(both.reshape(n_col * (piece + 8), n_labels), "col", n_col)
            own_part, degree = both[:piece], both[piece, :piece]
        else:
            own_part = scatter_sum(partial_value, "col", n_col)
        labels = 0.9 * own_part / degree[:, None] + 0.1 * seeded
    return labels


def solution(mesh):
    n_row, n_col = mesh.devices.shape
    fine = Mesh(mesh.devices.reshape(n_row // 8, 4, 2, n_col), DOCS)
    return jax.shard_map(
        local,
        mesh=fine,
        in_specs=(
            P(DOCS, None),
            P(DOCS),
            P(DOCS, None),
            P(DOCS),
            P(("zh", "x", "core"), None),
        ),
        out_specs=P(DOCS, None),
        check_vma=False,
    )
```

```python
import jax
import jax.numpy as jnp
from jax import lax
from jax.sharding import Mesh
from jax.sharding import PartitionSpec as P

ITERS = 3
CHIPS = ("zh", "x")
DOCS = ("zh", "x", "core", "col")


def gather_rows(x, axis, n):
    copies = jnp.broadcast_to(x[None], (n,) + x.shape)
    got = lax.all_to_all(copies, axis, 0, 0, tiled=False)
    return got.reshape((n * x.shape[0],) + x.shape[1:])


def gather_row_set(x, n_chips):
    copies = jnp.broadcast_to(x[None], (n_chips,) + x.shape)
    mine = lax.all_to_all(copies, CHIPS, 0, 0, tiled=False)
    other = lax.ppermute(mine, "core", [(0, 1), (1, 0)])
    core0 = lax.axis_index("core") == 0
    both = jnp.stack([jnp.where(core0, mine, other), jnp.where(core0, other, mine)], axis=1)
    return both.reshape((2 * n_chips * x.shape[0],) + x.shape[1:])


def scatter_sum(p, axis, n):
    chunk = p.shape[0] // n
    got = lax.all_to_all(p.reshape((n, chunk) + p.shape[1:]), axis, 0, 0, tiled=False)
    return jnp.sum(got, axis=0)


def local(embeddings, sharpness, soft_labels, seed_mask, tile_mask):
    n_chips = lax.axis_size(CHIPS)
    n_col = lax.axis_size("col")
    col_index = lax.axis_index("col")
    piece, width = embeddings.shape
    n_labels = soft_labels.shape[1]
    seeded = seed_mask.astype(jnp.float32)[:, None] * soft_labels
    squares = jnp.sum(embeddings * embeddings, axis=1)
    packed = jnp.concatenate([embeddings, sharpness[:, None], squares[:, None]], axis=1)
    col_pack = lax.all_gather(packed, ("zh", "x", "core"), axis=0, tiled=True)
    row_pack = gather_rows(packed, "col", n_col)
    col_labels = gather_row_set(seeded, n_chips)
    row_emb, row_width, row_squares = row_pack[:, :width], row_pack[:, width], row_pack[:, width + 1]
    col_emb, col_width, col_squares = col_pack[:, :width], col_pack[:, width], col_pack[:, width + 1]
    block_rows = row_emb.shape[0]
    col_rows = col_emb.shape[0]
    grouped = tile_mask.reshape(n_col, 2 * n_chips, n_col)
    chosen = lax.dynamic_index_in_dim(grouped, col_index, axis=2, keepdims=False)
    col_mask = jnp.broadcast_to(chosen[:, None, :, None], (n_col, piece, 2 * n_chips, piece))
    col_mask = col_mask.reshape(block_rows, col_rows).astype(jnp.float32)
    cross = jnp.dot(row_emb, col_emb.T, precision=lax.Precision.HIGHEST, preferred_element_type=jnp.float32)
    distance = row_squares[:, None] + col_squares[None, :] - 2.0 * cross
    weights = jnp.exp(-(distance * row_width[:, None] * col_width[None, :])) * col_mask
    degree = None
    labels = seeded
    for iteration in range(ITERS):
        if iteration > 0:
            col_labels = gather_row_set(labels, n_chips)
        partial_value = jnp.dot(
            weights, col_labels, precision=lax.Precision.HIGH, preferred_element_type=jnp.float32
        )
        if degree is None:
            row_sums = jnp.sum(weights, axis=1).reshape(n_col, 1, piece)
            row_sums = jnp.pad(row_sums, ((0, 0), (0, 7), (0, n_labels - piece)))
            both = jnp.concatenate([partial_value.reshape(n_col, piece, n_labels), row_sums], axis=1)
            both = scatter_sum(both.reshape(n_col * (piece + 8), n_labels), "col", n_col)
            own_part, degree = both[:piece], both[piece, :piece]
        else:
            own_part = scatter_sum(partial_value, "col", n_col)
        labels = 0.9 * own_part / degree[:, None] + 0.1 * seeded
    return labels


def solution(mesh):
    n_row, n_col = mesh.devices.shape
    fine = Mesh(mesh.devices.reshape(n_row // 8, 4, 2, n_col), DOCS)
    return jax.shard_map(
        local,
        mesh=fine,
        in_specs=(
            P(DOCS, None),
            P(DOCS),
            P(DOCS, None),
            P(DOCS),
            P(("zh", "x", "core"), None),
        ),
        out_specs=P(DOCS, None),
        check_vma=False,
    )
```

```python
import jax
import jax.numpy as jnp
from jax import lax
from jax.sharding import Mesh
from jax.sharding import PartitionSpec as P

ITERS = 3
CHIPS = ("zh", "x")
DOCS = ("zh", "x", "core", "col")


def gather_rows(x, axis, n):
    copies = jnp.broadcast_to(x[None], (n,) + x.shape)
    got = lax.all_to_all(copies, axis, 0, 0, tiled=False)
    return got.reshape((n * x.shape[0],) + x.shape[1:])


def swap_halves(mine):
    other = lax.ppermute(mine, "core", [(0, 1), (1, 0)])
    return jnp.concatenate([mine, other], axis=0)


def gather_row_set(x, n_chips):
    copies = jnp.broadcast_to(x[None], (n_chips,) + x.shape)
    mine = lax.all_to_all(copies, CHIPS, 0, 0, tiled=False)
    return swap_halves(mine).reshape((2 * n_chips * x.shape[0],) + x.shape[1:])


def scatter_sum(p, axis, n):
    chunk = p.shape[0] // n
    got = lax.all_to_all(p.reshape((n, chunk) + p.shape[1:]), axis, 0, 0, tiled=False)
    return jnp.sum(got, axis=0)


def local(embeddings, sharpness, soft_labels, seed_mask, tile_mask):
    n_chips = lax.axis_size(CHIPS)
    n_col = lax.axis_size("col")
    col_index = lax.axis_index("col")
    piece, width = embeddings.shape
    n_labels = soft_labels.shape[1]
    seeded = seed_mask.astype(jnp.float32)[:, None] * soft_labels
    squares = jnp.sum(embeddings * embeddings, axis=1)
    packed = jnp.concatenate([embeddings, sharpness[:, None], squares[:, None]], axis=1)
    col_pack = lax.all_gather(jnp.concatenate([packed, seeded], axis=1), "x", axis=0, tiled=True)
    col_pack = swap_halves(lax.all_gather(col_pack, "zh", axis=0, tiled=True))
    row_pack = gather_rows(packed, "col", n_col)
    row_emb, row_width, row_squares = row_pack[:, :width], row_pack[:, width], row_pack[:, width + 1]
    col_emb, col_width, col_squares = col_pack[:, :width], col_pack[:, width], col_pack[:, width + 1]
    col_labels = col_pack[:, width + 2:]
    block_rows = row_emb.shape[0]
    col_rows = col_emb.shape[0]
    grouped = tile_mask.reshape(n_col, n_chips, 2, n_col)
    chosen = lax.dynamic_index_in_dim(grouped, col_index, axis=3, keepdims=False)
    core = lax.axis_index("core")
    own_half = lax.dynamic_index_in_dim(chosen, core, axis=2, keepdims=False)
    other_half = lax.dynamic_index_in_dim(chosen, 1 - core, axis=2, keepdims=False)
    chosen = jnp.concatenate([own_half, other_half], axis=1)
    col_mask = jnp.broadcast_to(chosen[:, None, :, None], (n_col, piece, 2 * n_chips, piece))
    col_mask = col_mask.reshape(block_rows, col_rows).astype(jnp.float32)
    cross = jnp.dot(row_emb, col_emb.T, precision=lax.Precision.HIGHEST, preferred_element_type=jnp.float32)
    distance = row_squares[:, None] + col_squares[None, :] - 2.0 * cross
    weights = jnp.exp(-(distance * row_width[:, None] * col_width[None, :])) * col_mask
    degree = None
    labels = seeded
    for iteration in range(ITERS):
        if iteration > 0:
            col_labels = gather_row_set(labels, n_chips)
        partial_value = jnp.dot(
            weights, col_labels, precision=lax.Precision.HIGH, preferred_element_type=jnp.float32
        )
        if degree is None:
            row_sums = jnp.sum(weights, axis=1).reshape(n_col, 1, piece)
            row_sums = jnp.pad(row_sums, ((0, 0), (0, 7), (0, n_labels - piece)))
            both = jnp.concatenate([partial_value.reshape(n_col, piece, n_labels), row_sums], axis=1)
            both = scatter_sum(both.reshape(n_col * (piece + 8), n_labels), "col", n_col)
            own_part, degree = both[:piece], both[piece, :piece]
        else:
            own_part = scatter_sum(partial_value, "col", n_col)
        labels = 0.9 * own_part / degree[:, None] + 0.1 * seeded
    return labels


def solution(mesh):
    n_row, n_col = mesh.devices.shape
    fine = Mesh(mesh.devices.reshape(n_row // 8, 4, 2, n_col), DOCS)
    return jax.shard_map(
        local,
        mesh=fine,
        in_specs=(
            P(DOCS, None),
            P(DOCS),
            P(DOCS, None),
            P(DOCS),
            P(("zh", "x", "core"), None),
        ),
        out_specs=P(DOCS, None),
        check_vma=False,
    )
```

```python
import jax
import jax.numpy as jnp
from jax import lax
from jax.sharding import Mesh
from jax.sharding import PartitionSpec as P

ITERS = 3
CHIPS = ("zh", "x")
DOCS = ("zh", "x", "core", "col")


def gather_rows(x, axis, n):
    copies = jnp.broadcast_to(x[None], (n,) + x.shape)
    got = lax.all_to_all(copies, axis, 0, 0, tiled=False)
    return got.reshape((n * x.shape[0],) + x.shape[1:])


def gather_row_set(x, n_chips):
    copies = jnp.broadcast_to(x[None], (n_chips,) + x.shape)
    mine = lax.all_to_all(copies, CHIPS, 0, 0, tiled=False)
    other = lax.ppermute(mine, "core", [(0, 1), (1, 0)])
    core0 = lax.axis_index("core") == 0
    both = jnp.stack([jnp.where(core0, mine, other), jnp.where(core0, other, mine)], axis=1)
    return both.reshape((2 * n_chips * x.shape[0],) + x.shape[1:])


def scatter_sum(p, axis, n):
    chunk = p.shape[0] // n
    got = lax.all_to_all(p.reshape((n, chunk) + p.shape[1:]), axis, 0, 0, tiled=False)
    return jnp.sum(got, axis=0)


def local(embeddings, sharpness, soft_labels, seed_mask, tile_mask):
    n_chips = lax.axis_size(CHIPS)
    n_col = lax.axis_size("col")
    col_index = lax.axis_index("col")
    piece, width = embeddings.shape
    n_labels = soft_labels.shape[1]
    seeded = seed_mask.astype(jnp.float32)[:, None] * soft_labels
    packed = jnp.concatenate([embeddings, sharpness[:, None]], axis=1)
    col_pack = lax.all_gather(jnp.concatenate([packed, seeded], axis=1), ("zh", "x", "core"), axis=0, tiled=True)
    row_pack = gather_rows(packed, "col", n_col)
    row_emb, row_width = row_pack[:, :width], row_pack[:, width]
    col_emb, col_width = col_pack[:, :width], col_pack[:, width]
    col_labels = col_pack[:, width + 1:]
    row_squares = jnp.sum(row_emb * row_emb, axis=1)
    col_squares = jnp.sum(col_emb * col_emb, axis=1)
    block_rows = row_emb.shape[0]
    col_rows = col_emb.shape[0]
    grouped = tile_mask.reshape(n_col, 2 * n_chips, n_col)
    chosen = lax.dynamic_index_in_dim(grouped, col_index, axis=2, keepdims=False)
    col_mask = jnp.broadcast_to(chosen[:, None, :, None], (n_col, piece, 2 * n_chips, piece))
    col_mask = col_mask.reshape(block_rows, col_rows).astype(jnp.float32)
    cross = jnp.dot(row_emb, col_emb.T, precision=lax.Precision.HIGHEST, preferred_element_type=jnp.float32)
    distance = row_squares[:, None] + col_squares[None, :] - 2.0 * cross
    weights = jnp.exp(-(distance * row_width[:, None] * col_width[None, :])) * col_mask
    degree = None
    labels = seeded
    for iteration in range(ITERS):
        if iteration > 0:
            col_labels = gather_row_set(labels, n_chips)
        partial_value = jnp.dot(
            weights, col_labels, precision=lax.Precision.HIGH, preferred_element_type=jnp.float32
        )
        if degree is None:
            row_sums = jnp.sum(weights, axis=1).reshape(n_col, 1, piece)
            row_sums = jnp.pad(row_sums, ((0, 0), (0, 7), (0, n_labels - piece)))
            both = jnp.concatenate([partial_value.reshape(n_col, piece, n_labels), row_sums], axis=1)
            both = scatter_sum(both.reshape(n_col * (piece + 8), n_labels), "col", n_col)
            own_part, degree = both[:piece], both[piece, :piece]
        else:
            own_part = scatter_sum(partial_value, "col", n_col)
        labels = 0.9 * own_part / degree[:, None] + 0.1 * seeded
    return labels


def solution(mesh):
    n_row, n_col = mesh.devices.shape
    fine = Mesh(mesh.devices.reshape(n_row // 8, 4, 2, n_col), DOCS)
    return jax.shard_map(
        local,
        mesh=fine,
        in_specs=(
            P(DOCS, None),
            P(DOCS),
            P(DOCS, None),
            P(DOCS),
            P(("zh", "x", "core"), None),
        ),
        out_specs=P(DOCS, None),
        check_vma=False,
    )
```

```python
import jax
import jax.numpy as jnp
from jax import lax
from jax.sharding import Mesh
from jax.sharding import PartitionSpec as P

ITERS = 3
CHIPS = ("zh", "x")
DOCS = ("zh", "x", "core", "col")


def gather_rows(x, axis, n):
    copies = jnp.broadcast_to(x[None], (n,) + x.shape)
    got = lax.all_to_all(copies, axis, 0, 0, tiled=False)
    return got.reshape((n * x.shape[0],) + x.shape[1:])


def gather_row_set(x, n_chips):
    copies = jnp.broadcast_to(x[None], (n_chips,) + x.shape)
    mine = lax.all_to_all(copies, CHIPS, 0, 0, tiled=False)
    other = lax.ppermute(mine, "core", [(0, 1), (1, 0)])
    core0 = lax.axis_index("core") == 0
    both = jnp.stack([jnp.where(core0, mine, other), jnp.where(core0, other, mine)], axis=1)
    return both.reshape((2 * n_chips * x.shape[0],) + x.shape[1:])


def scatter_sum(p, axis, n):
    chunk = p.shape[0] // n
    got = lax.all_to_all(p.reshape((n, chunk) + p.shape[1:]), axis, 0, 0, tiled=False)
    return jnp.sum(got, axis=0)


def local(embeddings, sharpness, soft_labels, seed_mask, tile_mask):
    n_chips = lax.axis_size(CHIPS)
    n_col = lax.axis_size("col")
    col_index = lax.axis_index("col")
    piece, width = embeddings.shape
    n_labels = soft_labels.shape[1]
    seeded = seed_mask.astype(jnp.float32)[:, None] * soft_labels
    packed = jnp.concatenate([embeddings, sharpness[:, None]], axis=1)
    seed_column = seed_mask.astype(jnp.float32)[:, None]
    col_pack = lax.all_gather(
        jnp.concatenate([packed, seed_column, soft_labels], axis=1), ("zh", "x", "core"), axis=0, tiled=True
    )
    row_pack = gather_rows(packed, "col", n_col)
    row_emb, row_width = row_pack[:, :width], row_pack[:, width]
    col_emb, col_width = col_pack[:, :width], col_pack[:, width]
    col_labels = col_pack[:, width + 1:width + 2] * col_pack[:, width + 2:]
    row_squares = jnp.sum(row_emb * row_emb, axis=1)
    col_squares = jnp.sum(col_emb * col_emb, axis=1)
    block_rows = row_emb.shape[0]
    col_rows = col_emb.shape[0]
    grouped = tile_mask.reshape(n_col, 2 * n_chips, n_col)
    chosen = lax.dynamic_index_in_dim(grouped, col_index, axis=2, keepdims=False)
    col_mask = jnp.broadcast_to(chosen[:, None, :, None], (n_col, piece, 2 * n_chips, piece))
    col_mask = col_mask.reshape(block_rows, col_rows).astype(jnp.float32)
    cross = jnp.dot(row_emb, col_emb.T, precision=lax.Precision.HIGHEST, preferred_element_type=jnp.float32)
    distance = row_squares[:, None] + col_squares[None, :] - 2.0 * cross
    weights = jnp.exp(-(distance * row_width[:, None] * col_width[None, :])) * col_mask
    degree = None
    labels = seeded
    for iteration in range(ITERS):
        if iteration > 0:
            col_labels = gather_row_set(labels, n_chips)
        partial_value = jnp.dot(
            weights, col_labels, precision=lax.Precision.HIGH, preferred_element_type=jnp.float32
        )
        if degree is None:
            row_sums = jnp.sum(weights, axis=1).reshape(n_col, 1, piece)
            row_sums = jnp.pad(row_sums, ((0, 0), (0, 7), (0, n_labels - piece)))
            both = jnp.concatenate([partial_value.reshape(n_col, piece, n_labels), row_sums], axis=1)
            both = scatter_sum(both.reshape(n_col * (piece + 8), n_labels), "col", n_col)
            own_part, degree = both[:piece], both[piece, :piece]
        else:
            own_part = scatter_sum(partial_value, "col", n_col)
        labels = 0.9 * own_part / degree[:, None] + 0.1 * seeded
    return labels


def solution(mesh):
    n_row, n_col = mesh.devices.shape
    fine = Mesh(mesh.devices.reshape(n_row // 8, 4, 2, n_col), DOCS)
    return jax.shard_map(
        local,
        mesh=fine,
        in_specs=(
            P(DOCS, None),
            P(DOCS),
            P(DOCS, None),
            P(DOCS),
            P(("zh", "x", "core"), None),
        ),
        out_specs=P(DOCS, None),
        check_vma=False,
    )
```

```python
import jax
import jax.numpy as jnp
from jax import lax
from jax.sharding import Mesh
from jax.sharding import PartitionSpec as P

ITERS = 3
CHIPS = ("zh", "x")
DOCS = ("zh", "x", "core", "col")


def gather_rows(x, axis, n):
    copies = jnp.broadcast_to(x[None], (n,) + x.shape)
    got = lax.all_to_all(copies, axis, 0, 0, tiled=False)
    return got.reshape((n * x.shape[0],) + x.shape[1:])


def gather_row_set(x, n_chips):
    copies = jnp.broadcast_to(x[None], (n_chips,) + x.shape)
    mine = lax.all_to_all(copies, CHIPS, 0, 0, tiled=False)
    other = lax.ppermute(mine, "core", [(0, 1), (1, 0)])
    core0 = lax.axis_index("core") == 0
    both = jnp.stack([jnp.where(core0, mine, other), jnp.where(core0, other, mine)], axis=1)
    return both.reshape((2 * n_chips * x.shape[0],) + x.shape[1:])


def scatter_sum(p, axis, n):
    chunk = p.shape[0] // n
    got = lax.all_to_all(p.reshape((n, chunk) + p.shape[1:]), axis, 0, 0, tiled=False)
    return jnp.sum(got, axis=0)


def local(embeddings, sharpness, soft_labels, seed_mask, tile_mask):
    n_chips = lax.axis_size(CHIPS)
    n_col = lax.axis_size("col")
    col_index = lax.axis_index("col")
    piece, width = embeddings.shape
    n_labels = soft_labels.shape[1]
    seeded = seed_mask.astype(jnp.float32)[:, None] * soft_labels
    packed = jnp.concatenate([embeddings, sharpness[:, None]], axis=1)
    col_pack = lax.all_gather(jnp.concatenate([embeddings, seeded], axis=1), ("zh", "x", "core"), axis=0, tiled=True)
    row_pack = gather_rows(packed, "col", n_col)
    squares = jnp.sum(embeddings * embeddings, axis=1)
    col_scalars = gather_row_set(jnp.stack([sharpness, squares], axis=1), n_chips)
    row_emb, row_width = row_pack[:, :width], row_pack[:, width]
    col_emb, col_labels = col_pack[:, :width], col_pack[:, width:]
    col_width, col_squares = col_scalars[:, 0], col_scalars[:, 1]
    row_squares = jnp.sum(row_emb * row_emb, axis=1)
    block_rows = row_emb.shape[0]
    col_rows = col_emb.shape[0]
    grouped = tile_mask.reshape(n_col, 2 * n_chips, n_col)
    chosen = lax.dynamic_index_in_dim(grouped, col_index, axis=2, keepdims=False)
    col_mask = jnp.broadcast_to(chosen[:, None, :, None], (n_col, piece, 2 * n_chips, piece))
    col_mask = col_mask.reshape(block_rows, col_rows).astype(jnp.float32)
    cross = jnp.dot(row_emb, col_emb.T, precision=lax.Precision.HIGHEST, preferred_element_type=jnp.float32)
    distance = row_squares[:, None] + col_squares[None, :] - 2.0 * cross
    weights = jnp.exp(-(distance * row_width[:, None] * col_width[None, :])) * col_mask
    degree = None
    labels = seeded
    for iteration in range(ITERS):
        if iteration > 0:
            col_labels = gather_row_set(labels, n_chips)
        partial_value = jnp.dot(
            weights, col_labels, precision=lax.Precision.HIGH, preferred_element_type=jnp.float32
        )
        if degree is None:
            row_sums = jnp.sum(weights, axis=1).reshape(n_col, 1, piece)
            row_sums = jnp.pad(row_sums, ((0, 0), (0, 7), (0, n_labels - piece)))
            both = jnp.concatenate([partial_value.reshape(n_col, piece, n_labels), row_sums], axis=1)
            both = scatter_sum(both.reshape(n_col * (piece + 8), n_labels), "col", n_col)
            own_part, degree = both[:piece], both[piece, :piece]
        else:
            own_part = scatter_sum(partial_value, "col", n_col)
        labels = 0.9 * own_part / degree[:, None] + 0.1 * seeded
    return labels


def solution(mesh):
    n_row, n_col = mesh.devices.shape
    fine = Mesh(mesh.devices.reshape(n_row // 8, 4, 2, n_col), DOCS)
    return jax.shard_map(
        local,
        mesh=fine,
        in_specs=(
            P(DOCS, None),
            P(DOCS),
            P(DOCS, None),
            P(DOCS),
            P(("zh", "x", "core"), None),
        ),
        out_specs=P(DOCS, None),
        check_vma=False,
    )
```

```python
import jax
import jax.numpy as jnp
from jax import lax
from jax.sharding import Mesh
from jax.sharding import PartitionSpec as P

ITERS = 3
CHIPS = ("zh", "x")
DOCS = ("zh", "x", "core", "col")


def gather_rows(x, axis, n):
    copies = jnp.broadcast_to(x[None], (n,) + x.shape)
    got = lax.all_to_all(copies, axis, 0, 0, tiled=False)
    return got.reshape((n * x.shape[0],) + x.shape[1:])


def gather_row_set(x, n_chips):
    copies = jnp.broadcast_to(x[None], (n_chips,) + x.shape)
    mine = lax.all_to_all(copies, CHIPS, 0, 0, tiled=False)
    other = lax.ppermute(mine, "core", [(0, 1), (1, 0)])
    core0 = lax.axis_index("core") == 0
    both = jnp.stack([jnp.where(core0, mine, other), jnp.where(core0, other, mine)], axis=1)
    return both.reshape((2 * n_chips * x.shape[0],) + x.shape[1:])


def scatter_sum(p, axis, n):
    chunk = p.shape[0] // n
    got = lax.all_to_all(p.reshape((n, chunk) + p.shape[1:]), axis, 0, 0, tiled=False)
    return jnp.sum(got, axis=0)


def local(embeddings, sharpness, soft_labels, seed_mask, tile_mask):
    n_chips = lax.axis_size(CHIPS)
    n_col = lax.axis_size("col")
    col_index = lax.axis_index("col")
    piece, width = embeddings.shape
    n_labels = soft_labels.shape[1]
    seeded = seed_mask.astype(jnp.float32)[:, None] * soft_labels
    packed = jnp.concatenate([embeddings, sharpness[:, None]], axis=1)
    col_pack = lax.all_gather(jnp.concatenate([embeddings, soft_labels], axis=1), ("zh", "x", "core"), axis=0, tiled=True)
    row_pack = gather_rows(packed, "col", n_col)
    squares = jnp.sum(embeddings * embeddings, axis=1)
    col_scalars = gather_row_set(
        jnp.stack([sharpness, squares, seed_mask.astype(jnp.float32)], axis=1), n_chips
    )
    row_emb, row_width = row_pack[:, :width], row_pack[:, width]
    col_emb = col_pack[:, :width]
    col_width, col_squares = col_scalars[:, 0], col_scalars[:, 1]
    col_labels = col_scalars[:, 2:3] * col_pack[:, width:]
    row_squares = jnp.sum(row_emb * row_emb, axis=1)
    block_rows = row_emb.shape[0]
    col_rows = col_emb.shape[0]
    grouped = tile_mask.reshape(n_col, 2 * n_chips, n_col)
    chosen = lax.dynamic_index_in_dim(grouped, col_index, axis=2, keepdims=False)
    col_mask = jnp.broadcast_to(chosen[:, None, :, None], (n_col, piece, 2 * n_chips, piece))
    col_mask = col_mask.reshape(block_rows, col_rows).astype(jnp.float32)
    cross = jnp.dot(row_emb, col_emb.T, precision=lax.Precision.HIGHEST, preferred_element_type=jnp.float32)
    distance = row_squares[:, None] + col_squares[None, :] - 2.0 * cross
    weights = jnp.exp(-(distance * row_width[:, None] * col_width[None, :])) * col_mask
    degree = None
    labels = seeded
    for iteration in range(ITERS):
        if iteration > 0:
            col_labels = gather_row_set(labels, n_chips)
        partial_value = jnp.dot(
            weights, col_labels, precision=lax.Precision.HIGH, preferred_element_type=jnp.float32
        )
        if degree is None:
            row_sums = jnp.sum(weights, axis=1).reshape(n_col, 1, piece)
            row_sums = jnp.pad(row_sums, ((0, 0), (0, 7), (0, n_labels - piece)))
            both = jnp.concatenate([partial_value.reshape(n_col, piece, n_labels), row_sums], axis=1)
            both = scatter_sum(both.reshape(n_col * (piece + 8), n_labels), "col", n_col)
            own_part, degree = both[:piece], both[piece, :piece]
        else:
            own_part = scatter_sum(partial_value, "col", n_col)
        labels = 0.9 * own_part / degree[:, None] + 0.1 * seeded
    return labels


def solution(mesh):
    n_row, n_col = mesh.devices.shape
    fine = Mesh(mesh.devices.reshape(n_row // 8, 4, 2, n_col), DOCS)
    return jax.shard_map(
        local,
        mesh=fine,
        in_specs=(
            P(DOCS, None),
            P(DOCS),
            P(DOCS, None),
            P(DOCS),
            P(("zh", "x", "core"), None),
        ),
        out_specs=P(DOCS, None),
        check_vma=False,
    )
```
